32 devices in a mesh: row: 4 (over y, x), col: 8 (over z, core).
Axes of the slice: x: 2, y: 2, z: 4, core: 2. Of those that a mesh axis runs over, the one named last changes fastest.
Arguments:
- matrix_in: bfloat16 [2048, 2048], P('row', 'col'), as said below
- pattern: int32 [16, 16], replicated, may hold values from 0 to 1, as said below
Outputs:
- sign_step: float32 [2048, 2048], P('row', 'col')
The draws below stay inside these ranges and needn't reach their ends.
Inputs may be any that keep to these rules, and one draw needn't show every extreme that they name: `pattern`: symmetric, every diagonal block is 1, and every block (i, (i + 8) mod 16) is 1. `matrix_in`: exactly symmetric.
All inputs are finite; a program needn't handle non-finite values.
Results may differ from the reference program's by a relative error of at most 0.0029.
Values may be sent and summed in bfloat16 or wider, within the bound.
No kernel may reach another device: no remote copies, remote signals or barrier semaphores. Data moves between devices by JAX's collectives and lax.ppermute only.
A program may use at most 64 MiB of HBM per device.

```python
import math
import jax
import jax.numpy as jnp

B = 128
NB = 16
ORDER = 2048


def draw_pattern(key, part):
    block_index = jnp.arange(NB, dtype=jnp.int32)
    spacing = jnp.abs(block_index[:, None] - block_index[None, :])
    spacing = jnp.minimum(spacing, NB - spacing)
    draws_int = jax.random.randint(key, (NB, NB), 0, 64, dtype=jnp.int32)
    summed = draws_int + draws_int.T
    cutoff = 100 - 120 * spacing // NB
    chosen = (summed < cutoff) | (spacing == 0) | (spacing == NB // 2)
    return chosen.astype(jnp.int32)


def draw_matrix_in(key, part):
    key_noise = jax.random.fold_in(key, 11)
    key_size = jax.random.fold_in(key, 12)
    key_sign = jax.random.fold_in(key, 13)
    noise = jax.random.normal(key_noise, (ORDER, ORDER), jnp.float32)
    symmetric = (noise + noise.T) * 0.70710678
    spread = 1.0 / math.sqrt(ORDER)
    magnitude = jax.random.uniform(key_size, (ORDER,), jnp.float32, 0.3, 0.9)
    signs = (jax.random.randint(key_sign, (ORDER,), 0, 2, dtype=jnp.int32) * 2 - 1).astype(jnp.float32)
    identity = jnp.eye(ORDER, dtype=jnp.float32)
    return (symmetric * spread + identity * (magnitude * signs)[None, :]).astype(jnp.bfloat16)


def setup_inputs(seed: int = 0) -> dict:
    arg_keys = jax.random.split(jax.random.key(seed), 3)
    return {
        "matrix_in": draw_matrix_in(jax.random.fold_in(arg_keys[2], 71), 0),
        "pattern": draw_pattern(jax.random.fold_in(arg_keys[2], 71), 0),
    }


def expand_blocks(pattern):
    return jnp.repeat(jnp.repeat(pattern, B, axis=0), B, axis=1)


def reference(matrix_in, pattern):
    kept_mask = expand_blocks(pattern)
    masked = matrix_in * kept_mask.astype(jnp.bfloat16)
    square = jnp.dot(masked, masked, preferred_element_type=jnp.float32)
    filtered = (kept_mask.astype(jnp.float32) * square).astype(jnp.bfloat16)
    cubic = jnp.dot(masked, filtered, preferred_element_type=jnp.float32)
    return kept_mask.astype(jnp.float32) * (1.5 * masked.astype(jnp.float32) - 0.5 * cubic)
```

```python
import jax
import jax.numpy as jnp
from jax import lax
from jax.sharding import PartitionSpec as P

B = 128


def _xor_gather(x, axis, n, index, stride=1):
    pieces = [x]
    for k in range(1, n):
        d = k * stride
        perm = [(i, i ^ d) for i in range(n * stride)]
        pieces.append(lax.ppermute(x, axis, perm))
    stacked = jnp.stack(pieces)
    order = jnp.arange(n, dtype=jnp.int32) ^ index
    return jnp.take(stacked, order, axis=0)


def make_body(n_row, n_col):
    n_z = n_col // 2

    def body(matrix_in, pattern):
        rows, cols = matrix_in.shape
        block_rows = rows // B
        block_cols = cols // B
        row_index = lax.axis_index("row")
        col_index = lax.axis_index("col")
        z_index = col_index // 2
        core = col_index % 2
        local_blocks = lax.dynamic_slice(
            pattern, (row_index * block_rows, col_index * block_cols), (block_rows, block_cols)
        )
        local_mask = jnp.repeat(jnp.repeat(local_blocks, B, axis=0), B, axis=1)
        masked = matrix_in * local_mask.astype(jnp.bfloat16)

        col_panel = _xor_gather(masked, "row", n_row, row_index).reshape(n_row * rows, cols)

        own = _xor_gather(masked, "col", n_z, z_index, stride=2)
        other = lax.ppermute(own, "col", [(i, i ^ 1) for i in range(n_col)])
        first = jnp.where(core == 0, own, other)
        second = jnp.where(core == 0, other, own)
        row_panel = jnp.stack([first, second], axis=1)
        row_panel = jnp.transpose(row_panel, (2, 0, 1, 3)).reshape(rows, n_col * cols)

        square = jnp.dot(row_panel, col_panel, preferred_element_type=jnp.float32)
        mask_float = local_mask.astype(jnp.float32)
        filtered = (mask_float * square).astype(jnp.bfloat16)
        f_panel = _xor_gather(filtered, "row", n_row, row_index).reshape(n_row * rows, cols)
        cubic = jnp.dot(row_panel, f_panel, preferred_element_type=jnp.float32)
        return mask_float * (1.5 * masked.astype(jnp.float32) - 0.5 * cubic)

    return body


def solution(mesh):
    return jax.shard_map(
        make_body(mesh.shape["row"], mesh.shape["col"]),
        mesh=mesh,
        in_specs=(P("row", "col"), P()),
        out_specs=P("row", "col"),
        check_vma=False,
    )
```

```python
import jax
import jax.numpy as jnp
from jax import lax
from jax.sharding import PartitionSpec as P

B = 128


def _swap(x, axis, size, d):
    return lax.ppermute(x, axis, [(i, i ^ d) for i in range(size)])


def make_body(n_row, n_col):
    n_z = n_col // 2

    def body(matrix_in, pattern):
        rows, cols = matrix_in.shape
        ratio = rows // cols
        block_rows = rows // B
        block_cols = cols // B
        row_index = lax.axis_index("row")
        col_index = lax.axis_index("col")
        local_blocks = lax.dynamic_slice(
            pattern, (row_index * block_rows, col_index * block_cols), (block_rows, block_cols)
        )
        local_mask = jnp.repeat(jnp.repeat(local_blocks, B, axis=0), B, axis=1)
        masked = matrix_in * local_mask.astype(jnp.bfloat16)

        row_pieces = [None] * n_col
        row_pieces[0] = masked
        row_pieces[1] = _swap(masked, "col", n_col, 1)
        for k in range(1, n_z):
            piece = _swap(masked, "col", n_col, 2 * k)
            row_pieces[2 * k] = piece
            row_pieces[2 * k + 1] = _swap(piece, "col", n_col, 1)

        col_pieces = [masked] + [_swap(masked, "row", n_row, k) for k in range(1, n_row)]

        slots = jnp.arange(n_col, dtype=jnp.int32) ^ col_index
        sub_index = ((slots // ratio) ^ row_index) * ratio + slots % ratio

        def in_slot_order(pieces):
            stacked = jnp.stack(pieces).reshape(n_row * ratio, cols, cols)
            return jnp.take(stacked, sub_index, axis=0)

        row_stack = jnp.stack(row_pieces)
        col_slot = in_slot_order(col_pieces)
        square = jnp.einsum(
            "tmj,tjn->mn", row_stack, col_slot, preferred_element_type=jnp.float32
        )
        mask_float = local_mask.astype(jnp.float32)
        filtered = (mask_float * square).astype(jnp.bfloat16)
        f_pieces = [filtered] + [_swap(filtered, "row", n_row, k) for k in range(1, n_row)]
        f_slot = in_slot_order(f_pieces)
        cubic = jnp.einsum("tmj,tjn->mn", row_stack, f_slot, preferred_element_type=jnp.float32)
        return mask_float * (1.5 * masked.astype(jnp.float32) - 0.5 * cubic)

    return body


def solution(mesh):
    return jax.shard_map(
        make_body(mesh.shape["row"], mesh.shape["col"]),
        mesh=mesh,
        in_specs=(P("row", "col"), P()),
        out_specs=P("row", "col"),
        check_vma=False,
    )
```

```python
import jax
import jax.numpy as jnp
from jax import lax
from jax.sharding import PartitionSpec as P

B = 128


def _swap(x, axis, size, d):
    return lax.ppermute(x, axis, [(i, i ^ d) for i in range(size)])


def make_body(n_row, n_col):
    n_z = n_col // 2

    def body(matrix_in, pattern):
        rows, cols = matrix_in.shape
        ratio = rows // cols
        block_rows = rows // B
        block_cols = cols // B
        row_index = lax.axis_index("row")
        col_index = lax.axis_index("col")
        z_index = col_index // 2
        core = col_index % 2
        local_blocks = lax.dynamic_slice(
            pattern, (row_index * block_rows, col_index * block_cols), (block_rows, block_cols)
        )
        local_mask = jnp.repeat(jnp.repeat(local_blocks, B, axis=0), B, axis=1)
        masked = matrix_in * local_mask.astype(jnp.bfloat16)

        col_pieces = [masked] + [_swap(masked, "row", n_row, k) for k in range(1, n_row)]

        own = [(masked, z_index)]
        to_right, to_left = masked, masked
        for s in range(1, n_z):
            right_pairs = [(2 * (z - 1) + c, 2 * z + c) for z in range(s, n_z) for c in range(2)]
            left_pairs = [(2 * (z + 1) + c, 2 * z + c) for z in range(0, n_z - s) for c in range(2)]
            to_right = lax.ppermute(to_right, "col", right_pairs)
            to_left = lax.ppermute(to_left, "col", left_pairs)
            own.append((to_right, z_index - s))
            own.append((to_left, z_index + s))
        slots = [(p, 2 * zz + core) for p, zz in own]
        slots += [(_swap(p, "col", n_col, 1), 2 * zz + 1 - core) for p, zz in own]

        block = jnp.stack([jnp.clip(c, 0, n_col - 1) for _, c in slots])
        sub_index = ((block // ratio) ^ row_index) * ratio + block % ratio
        row_cat = jnp.concatenate([p for p, _ in slots], axis=1)

        def in_slot_order(pieces):
            stacked = jnp.stack(pieces).reshape(n_row * ratio, cols, cols)
            return jnp.take(stacked, sub_index, axis=0).reshape(len(slots) * cols, cols)

        square = jnp.dot(row_cat, in_slot_order(col_pieces), preferred_element_type=jnp.float32)
        mask_float = local_mask.astype(jnp.float32)
        filtered = (mask_float * square).astype(jnp.bfloat16)
        f_pieces = [filtered] + [_swap(filtered, "row", n_row, k) for k in range(1, n_row)]
        cubic = jnp.dot(row_cat, in_slot_order(f_pieces), preferred_element_type=jnp.float32)
        return mask_float * (1.5 * masked.astype(jnp.float32) - 0.5 * cubic)

    return body


def solution(mesh):
    return jax.shard_map(
        make_body(mesh.shape["row"], mesh.shape["col"]),
        mesh=mesh,
        in_specs=(P("row", "col"), P()),
        out_specs=P("row", "col"),
        check_vma=False,
    )
```

```python
import jax
import jax.numpy as jnp
from jax import lax
from jax.sharding import PartitionSpec as P

B = 128


def _swap(x, axis, size, d):
    return lax.ppermute(x, axis, [(i, i ^ d) for i in range(size)])


def make_body(n_row, n_col):
    n_z = n_col // 2

    def body(matrix_in, pattern):
        rows, cols = matrix_in.shape
        ratio = rows // cols
        block_rows = rows // B
        block_cols = cols // B
        row_index = lax.axis_index("row")
        col_index = lax.axis_index("col")
        local_blocks = lax.dynamic_slice(
            pattern, (row_index * block_rows, col_index * block_cols), (block_rows, block_cols)
        )
        local_mask = jnp.repeat(jnp.repeat(local_blocks, B, axis=0), B, axis=1)
        masked = matrix_in * local_mask.astype(jnp.bfloat16)

        row_pieces = [None] * n_col
        row_pieces[0] = masked
        row_pieces[1] = _swap(masked, "col", n_col, 1)
        for k in range(1, n_z):
            piece = _swap(masked, "col", n_col, 2 * k)
            row_pieces[2 * k] = piece
            row_pieces[2 * k + 1] = _swap(piece, "col", n_col, 1)

        col_pieces = [masked] + [_swap(masked, "row", n_row, k) for k in range(1, n_row)]

        slots = jnp.arange(n_col, dtype=jnp.int32) ^ col_index
        sub_index = ((slots // ratio) ^ row_index) * ratio + slots % ratio

        def in_slot_order(pieces):
            stacked = jnp.stack(pieces).reshape(n_row * ratio, cols, cols)
            return jnp.take(stacked, sub_index, axis=0).reshape(n_col * cols, cols)

        row_cat = jnp.concatenate(row_pieces, axis=1)
        square = jnp.dot(row_cat, in_slot_order(col_pieces), preferred_element_type=jnp.float32)
        mask_float = local_mask.astype(jnp.float32)
        filtered = (mask_float * square).astype(jnp.bfloat16)
        f_pieces = [filtered] + [_swap(filtered, "row", n_row, k) for k in range(1, n_row)]
        f_slot = in_slot_order(f_pieces)
        cubic = jnp.dot(row_cat, f_slot, preferred_element_type=jnp.float32)
        return mask_float * (1.5 * masked.astype(jnp.float32) - 0.5 * cubic)

    return body


def solution(mesh):
    return jax.shard_map(
        make_body(mesh.shape["row"], mesh.shape["col"]),
        mesh=mesh,
        in_specs=(P("row", "col"), P()),
        out_specs=P("row", "col"),
        check_vma=False,
    )
```

```python
import jax
import jax.numpy as jnp
from jax import lax
from jax.sharding import PartitionSpec as P

B = 128


def _swap(x, axis, size, d):
    return lax.ppermute(x, axis, [(i, i ^ d) for i in range(size)])


def make_body(n_row, n_col):
    n_z = n_col // 2

    def body(matrix_in, pattern):
        rows, cols = matrix_in.shape
        ratio = rows // cols
        block_rows = rows // B
        block_cols = cols // B
        row_index = lax.axis_index("row")
        col_index = lax.axis_index("col")
        local_blocks = lax.dynamic_slice(
            pattern, (row_index * block_rows, col_index * block_cols), (block_rows, block_cols)
        )
        keep = local_blocks.reshape(block_rows, 1, block_cols, 1) != 0

        def apply_mask(x):
            x4 = x.reshape(block_rows, B, block_cols, B)
            return jnp.where(keep, x4, jnp.zeros_like(x4)).reshape(rows, cols)

        masked = apply_mask(matrix_in)

        row_pieces = [None] * n_col
        row_pieces[0] = masked
        row_pieces[1] = _swap(masked, "col", n_col, 1)
        for k in range(1, n_z):
            piece = _swap(masked, "col", n_col, 2 * k)
            row_pieces[2 * k] = piece
            row_pieces[2 * k + 1] = _swap(piece, "col", n_col, 1)

        col_pieces = [masked] + [_swap(masked, "row", n_row, k) for k in range(1, n_row)]

        slots = jnp.arange(n_col, dtype=jnp.int32) ^ col_index
        sub_index = ((slots // ratio) ^ row_index) * ratio + slots % ratio

        def in_slot_order(pieces):
            stacked = jnp.stack(pieces).reshape(n_row * ratio, cols, cols)
            return jnp.take(stacked, sub_index, axis=0).reshape(n_col * cols, cols)

        row_cat = jnp.concatenate(row_pieces, axis=1)
        square = jnp.dot(row_cat, in_slot_order(col_pieces), preferred_element_type=jnp.float32)
        filtered = apply_mask(square).astype(jnp.bfloat16)
        f_pieces = [filtered] + [_swap(filtered, "row", n_row, k) for k in range(1, n_row)]
        f_slot = in_slot_order(f_pieces)
        cubic = jnp.dot(row_cat, f_slot, preferred_element_type=jnp.float32)
        return apply_mask(1.5 * masked.astype(jnp.float32) - 0.5 * cubic)

    return body


def solution(mesh):
    return jax.shard_map(
        make_body(mesh.shape["row"], mesh.shape["col"]),
        mesh=mesh,
        in_specs=(P("row", "col"), P()),
        out_specs=P("row", "col"),
        check_vma=False,
    )
```

```python
import jax
import jax.numpy as jnp
from jax import lax
from jax.sharding import PartitionSpec as P

B = 128


def _swap(x, axis, size, d):
    return lax.ppermute(x, axis, [(i, i ^ d) for i in range(size)])


def make_body(n_row, n_col):
    n_z = n_col // 2

    def body(matrix_in, pattern):
        rows, cols = matrix_in.shape
        ratio = rows // cols
        block_rows = rows // B
        block_cols = cols // B
        row_index = lax.axis_index("row")
        col_index = lax.axis_index("col")
        local_blocks = lax.dynamic_slice(
            pattern, (row_index * block_rows, col_index * block_cols), (block_rows, block_cols)
        )
        local_mask = jnp.repeat(jnp.repeat(local_blocks, B, axis=0), B, axis=1)
        masked = matrix_in * local_mask.astype(jnp.bfloat16)

        col_pieces = [masked] + [_swap(masked, "row", n_row, j) for j in range(1, n_row)]

        late, _ = lax.optimization_barrier((masked, col_pieces[1]))
        own = jnp.concatenate(
            [masked]
            + [_swap(late if k == 1 else masked, "col", n_col, 2 * k) for k in range(1, n_z)],
            axis=1,
        )
        row_cat = jnp.concatenate([own, _swap(own, "col", n_col, 1)], axis=1)

        members = jnp.arange(n_z, dtype=jnp.int32) * 2
        slots = jnp.concatenate([members, members + 1]) ^ col_index
        sub_index = ((slots // ratio) ^ row_index) * ratio + slots % ratio

        def in_slot_order(pieces):
            stacked = jnp.stack(pieces).reshape(n_row * ratio, cols, cols)
            return jnp.take(stacked, sub_index, axis=0).reshape(n_col * cols, cols)

        square = jnp.dot(row_cat, in_slot_order(col_pieces), preferred_element_type=jnp.float32)
        mask_float = local_mask.astype(jnp.float32)
        filtered = (mask_float * square).astype(jnp.bfloat16)
        f_pieces = [filtered] + [_swap(filtered, "row", n_row, k) for k in range(1, n_row)]
        f_slot = in_slot_order(f_pieces)
        cubic = jnp.dot(row_cat, f_slot, preferred_element_type=jnp.float32)
        return mask_float * (1.5 * masked.astype(jnp.float32) - 0.5 * cubic)

    return body


def solution(mesh):
    return jax.shard_map(
        make_body(mesh.shape["row"], mesh.shape["col"]),
        mesh=mesh,
        in_specs=(P("row", "col"), P()),
        out_specs=P("row", "col"),
        check_vma=False,
    )
```

```python
import jax
import jax.numpy as jnp
from jax import lax
from jax.sharding import PartitionSpec as P

B = 128


def _swap(x, axis, size, d):
    return lax.ppermute(x, axis, [(i, i ^ d) for i in range(size)])


def make_body(n_row, n_col):
    n_z = n_col // 2

    def body(matrix_in, pattern):
        rows, cols = matrix_in.shape
        ratio = rows // cols
        block_rows = rows // B
        block_cols = cols // B
        row_index = lax.axis_index("row")
        col_index = lax.axis_index("col")
        local_blocks = lax.dynamic_slice(
            pattern, (row_index * block_rows, col_index * block_cols), (block_rows, block_cols)
        )
        local_mask = jnp.repeat(jnp.repeat(local_blocks, B, axis=0), B, axis=1)
        masked = matrix_in * local_mask.astype(jnp.bfloat16)

        col_pieces = [masked] + [_swap(masked, "row", n_row, j) for j in range(1, n_row)]

        late, _ = lax.optimization_barrier((masked, col_pieces[1]))
        row_pieces = [None] * n_col
        row_pieces[0] = masked
        row_pieces[1] = _swap(late, "col", n_col, 1)
        for k in range(1, n_z):
            piece = _swap(late if k == 1 else masked, "col", n_col, 2 * k)
            row_pieces[2 * k] = piece
            row_pieces[2 * k + 1] = _swap(piece, "col", n_col, 1)

        slots = jnp.arange(n_col, dtype=jnp.int32) ^ col_index
        sub_index = ((slots // ratio) ^ row_index) * ratio + slots % ratio

        def in_slot_order(pieces):
            stacked = jnp.stack(pieces).reshape(n_row * ratio, cols, cols)
            return jnp.take(stacked, sub_index, axis=0).reshape(n_col * cols, cols)

        row_cat = jnp.concatenate(row_pieces, axis=1)
        square = jnp.dot(row_cat, in_slot_order(col_pieces), preferred_element_type=jnp.float32)
        mask_float = local_mask.astype(jnp.float32)
        filtered = (mask_float * square).astype(jnp.bfloat16)
        f_pieces = [filtered] + [_swap(filtered, "row", n_row, k) for k in range(1, n_row)]
        f_slot = in_slot_order(f_pieces)
        cubic = jnp.dot(row_cat, f_slot, preferred_element_type=jnp.float32)
        return mask_float * (1.5 * masked.astype(jnp.float32) - 0.5 * cubic)

    return body


def solution(mesh):
    return jax.shard_map(
        make_body(mesh.shape["row"], mesh.shape["col"]),
        mesh=mesh,
        in_specs=(P("row", "col"), P()),
        out_specs=P("row", "col"),
        check_vma=False,
    )
```

```python
import jax
import jax.numpy as jnp
from jax import lax
from jax.sharding import PartitionSpec as P

B = 128


def _swap(x, axis, size, d):
    return lax.ppermute(x, axis, [(i, i ^ d) for i in range(size)])


def make_body(n_row, n_col):
    n_z = n_col // 2

    def body(matrix_in, pattern):
        rows, cols = matrix_in.shape
        ratio = rows // cols
        block_rows = rows // B
        block_cols = cols // B
        row_index = lax.axis_index("row")
        col_index = lax.axis_index("col")
        local_blocks = lax.dynamic_slice(
            pattern, (row_index * block_rows, col_index * block_cols), (block_rows, block_cols)
        )
        local_mask = jnp.repeat(jnp.repeat(local_blocks, B, axis=0), B, axis=1)
        masked = matrix_in * local_mask.astype(jnp.bfloat16)

        col_pieces = [masked] + [_swap(masked, "row", n_row, j) for j in range(1, n_row)]

        late, _ = lax.optimization_barrier((masked, col_pieces[1]))

        slots = jnp.arange(n_col, dtype=jnp.int32) ^ col_index
        sub_index = ((slots // ratio) ^ row_index) * ratio + slots % ratio

        def in_slot_order(pieces):
            stacked = jnp.stack(pieces).reshape(n_row * ratio, cols, cols)
            return jnp.take(stacked, sub_index, axis=0).reshape(n_col * cols, cols)

        col_slot = None
        mask_float = local_mask.astype(jnp.float32)
        waves = 2 if rows % (2 * B) == 0 else 1
        half = rows // waves
        row_cats, f_waves = [], []
        previous = None
        for w in range(waves):
            part = masked[w * half:(w + 1) * half]
            early = late[w * half:(w + 1) * half]
            if previous is not None:
                part, _ = lax.optimization_barrier((part, previous))
                early = part
            pieces = [None] * n_col
            pieces[0] = part
            pieces[1] = _swap(early, "col", n_col, 1)
            for k in range(1, n_z):
                piece = _swap(early if k == 1 else part, "col", n_col, 2 * k)
                pieces[2 * k] = piece
                pieces[2 * k + 1] = _swap(piece, "col", n_col, 1)
            row_cat = jnp.concatenate(pieces, axis=1)
            row_cats.append(row_cat)
            if col_slot is None:
                col_slot = in_slot_order(col_pieces)
            square = jnp.dot(row_cat, col_slot, preferred_element_type=jnp.float32)
            filtered = (mask_float[w * half:(w + 1) * half] * square).astype(jnp.bfloat16)
            previous = filtered
            f_wave = [filtered] + [None] * (n_row - 1)
            if w + 1 < waves:
                step = 1
                while step < n_row:
                    got = _swap(jnp.stack(f_wave[:step]), "row", n_row, step)
                    for j in range(step):
                        f_wave[j ^ step] = got[j]
                    step *= 2
            else:
                for j in range(1, n_row):
                    f_wave[j] = _swap(filtered, "row", n_row, j)
            f_waves.append(f_wave)

        f_pieces = [jnp.concatenate([fw[j] for fw in f_waves], axis=0) for j in range(n_row)]
        f_slot = in_slot_order(f_pieces)
        cubic = jnp.concatenate(
            [jnp.dot(rc, f_slot, preferred_element_type=jnp.float32) for rc in row_cats], axis=0
        )
        return mask_float * (1.5 * masked.astype(jnp.float32) - 0.5 * cubic)

    return body


def solution(mesh):
    return jax.shard_map(
        make_body(mesh.shape["row"], mesh.shape["col"]),
        mesh=mesh,
        in_specs=(P("row", "col"), P()),
        out_specs=P("row", "col"),
        check_vma=False,
    )
```

```python
import jax
import jax.numpy as jnp
from jax import lax
from jax.sharding import PartitionSpec as P

B = 128


def _swap(x, axis, size, d):
    return lax.ppermute(x, axis, [(i, i ^ d) for i in range(size)])


def make_body(n_row, n_col):
    n_z = n_col // 2

    def body(matrix_in, pattern):
        rows, cols = matrix_in.shape
        ratio = rows // cols
        block_rows = rows // B
        block_cols = cols // B
        row_index = lax.axis_index("row")
        col_index = lax.axis_index("col")
        local_blocks = lax.dynamic_slice(
            pattern, (row_index * block_rows, col_index * block_cols), (block_rows, block_cols)
        )
        local_mask = jnp.repeat(jnp.repeat(local_blocks, B, axis=0), B, axis=1)
        masked = matrix_in * local_mask.astype(jnp.bfloat16)

        first = _swap(masked, "row", n_row, 1)
        late, _ = lax.optimization_barrier((masked, first))
        col_pieces = [masked, first] + [_swap(late, "row", n_row, j) for j in range(2, n_row)]

        row_pieces = [None] * n_col
        row_pieces[0] = masked
        row_pieces[1] = _swap(late, "col", n_col, 1)
        for k in range(1, n_z):
            piece = _swap(late if k == 1 else masked, "col", n_col, 2 * k)
            row_pieces[2 * k] = piece
            row_pieces[2 * k + 1] = _swap(piece, "col", n_col, 1)

        slots = jnp.arange(n_col, dtype=jnp.int32) ^ col_index
        sub_index = ((slots // ratio) ^ row_index) * ratio + slots % ratio

        def in_slot_order(pieces):
            stacked = jnp.stack(pieces).reshape(n_row * ratio, cols, cols)
            return jnp.take(stacked, sub_index, axis=0).reshape(n_col * cols, cols)

        row_cat = jnp.concatenate(row_pieces, axis=1)
        square = jnp.dot(row_cat, in_slot_order(col_pieces), preferred_element_type=jnp.float32)
        mask_float = local_mask.astype(jnp.float32)
        filtered = (mask_float * square).astype(jnp.bfloat16)
        f_pieces = [filtered] + [_swap(filtered, "row", n_row, k) for k in range(1, n_row)]
        f_slot = in_slot_order(f_pieces)
        cubic = jnp.dot(row_cat, f_slot, preferred_element_type=jnp.float32)
        return mask_float * (1.5 * masked.astype(jnp.float32) - 0.5 * cubic)

    return body


def solution(mesh):
    return jax.shard_map(
        make_body(mesh.shape["row"], mesh.shape["col"]),
        mesh=mesh,
        in_specs=(P("row", "col"), P()),
        out_specs=P("row", "col"),
        check_vma=False,
    )
```

```python
import jax
import jax.numpy as jnp
from jax import lax
from jax.sharding import PartitionSpec as P

B = 128


def _swap(x, axis, size, d):
    return lax.ppermute(x, axis, [(i, i ^ d) for i in range(size)])


def make_body(n_row, n_col):
    n_z = n_col // 2

    def body(matrix_in, pattern):
        rows, cols = matrix_in.shape
        ratio = rows // cols
        block_rows = rows // B
        block_cols = cols // B
        row_index = lax.axis_index("row")
        col_index = lax.axis_index("col")
        local_blocks = lax.dynamic_slice(
            pattern, (row_index * block_rows, col_index * block_cols), (block_rows, block_cols)
        )
        local_mask = jnp.repeat(jnp.repeat(local_blocks, B, axis=0), B, axis=1)
        masked = matrix_in * local_mask.astype(jnp.bfloat16)

        row_pieces = [None] * n_col
        row_pieces[0] = masked
        for k in range(1, n_z):
            row_pieces[2 * k] = _swap(masked, "col", n_col, 2 * k)
        late = masked
        if n_z > 1:
            late, _ = lax.optimization_barrier((masked, row_pieces[2]))
        row_pieces[1] = _swap(late, "col", n_col, 1)
        for k in range(1, n_z):
            row_pieces[2 * k + 1] = _swap(row_pieces[2 * k], "col", n_col, 1)

        col_pieces = [masked] + [_swap(late, "row", n_row, j) for j in range(1, n_row)]

        slots = jnp.arange(n_col, dtype=jnp.int32) ^ col_index
        sub_index = ((slots // ratio) ^ row_index) * ratio + slots % ratio

        def in_slot_order(pieces):
            stacked = jnp.stack(pieces).reshape(n_row * ratio, cols, cols)
            return jnp.take(stacked, sub_index, axis=0).reshape(n_col * cols, cols)

        row_cat = jnp.concatenate(row_pieces, axis=1)
        square = jnp.dot(row_cat, in_slot_order(col_pieces), preferred_element_type=jnp.float32)
        mask_float = local_mask.astype(jnp.float32)
        filtered = (mask_float * square).astype(jnp.bfloat16)
        f_pieces = [filtered] + [_swap(filtered, "row", n_row, k) for k in range(1, n_row)]
        f_slot = in_slot_order(f_pieces)
        cubic = jnp.dot(row_cat, f_slot, preferred_element_type=jnp.float32)
        return mask_float * (1.5 * masked.astype(jnp.float32) - 0.5 * cubic)

    return body


def solution(mesh):
    return jax.shard_map(
        make_body(mesh.shape["row"], mesh.shape["col"]),
        mesh=mesh,
        in_specs=(P("row", "col"), P()),
        out_specs=P("row", "col"),
        check_vma=False,
    )
```

```python
import jax
import jax.numpy as jnp
from jax import lax
from jax.sharding import PartitionSpec as P

B = 128


def _swap(x, axis, size, d):
    return lax.ppermute(x, axis, [(i, i ^ d) for i in range(size)])


def make_body(n_row, n_col):
    n_z = n_col // 2

    def body(matrix_in, pattern):
        rows, cols = matrix_in.shape
        ratio = rows // cols
        block_rows = rows // B
        block_cols = cols // B
        row_index = lax.axis_index("row")
        col_index = lax.axis_index("col")
        local_blocks = lax.dynamic_slice(
            pattern, (row_index * block_rows, col_index * block_cols), (block_rows, block_cols)
        )
        local_mask = jnp.repeat(jnp.repeat(local_blocks, B, axis=0), B, axis=1)
        masked = matrix_in * local_mask.astype(jnp.bfloat16)
        sent = matrix_in

        col_pieces = [sent] + [_swap(sent, "row", n_row, j) for j in range(1, n_row)]

        late, _ = lax.optimization_barrier((sent, col_pieces[1]))
        row_pieces = [None] * n_col
        row_pieces[0] = sent
        row_pieces[1] = _swap(late, "col", n_col, 1)
        for k in range(1, n_z):
            piece = _swap(late if k == 1 else sent, "col", n_col, 2 * k)
            row_pieces[2 * k] = piece
            row_pieces[2 * k + 1] = _swap(piece, "col", n_col, 1)

        slots = jnp.arange(n_col, dtype=jnp.int32) ^ col_index
        sub_index = ((slots // ratio) ^ row_index) * ratio + slots % ratio

        def in_slot_order(pieces):
            stacked = jnp.stack(pieces).reshape(n_row * ratio, cols, cols)
            return jnp.take(stacked, sub_index, axis=0).reshape(n_col * cols, cols)

        row_cat = jnp.concatenate(row_pieces, axis=1)
        halves = jnp.arange(block_cols, dtype=jnp.int32)
        slot_blocks = (slots[:, None] * block_cols + halves[None, :]).reshape(-1)
        own_rows = lax.dynamic_slice_in_dim(pattern, row_index * block_rows, block_rows, 0)
        row_keep = jnp.take(own_rows, slot_blocks, axis=1).astype(jnp.bfloat16)
        own_cols = lax.dynamic_slice_in_dim(pattern, col_index * block_cols, block_cols, 1)
        col_keep = jnp.take(own_cols, slot_blocks, axis=0).astype(jnp.bfloat16)
        n_slot_blocks = n_col * block_cols
        row_cat = (
            row_cat.reshape(block_rows, B, n_slot_blocks, B) * row_keep[:, None, :, None]
        ).reshape(rows, n_col * cols)
        col_slot = in_slot_order(col_pieces)
        col_slot = (
            col_slot.reshape(n_slot_blocks, B, block_cols, B) * col_keep[:, None, :, None]
        ).reshape(n_col * cols, cols)
        square = jnp.dot(row_cat, col_slot, preferred_element_type=jnp.float32)
        mask_float = local_mask.astype(jnp.float32)
        filtered = (mask_float * square).astype(jnp.bfloat16)
        f_pieces = [filtered] + [_swap(filtered, "row", n_row, k) for k in range(1, n_row)]
        f_slot = in_slot_order(f_pieces)
        cubic = jnp.dot(row_cat, f_slot, preferred_element_type=jnp.float32)
        return mask_float * (1.5 * masked.astype(jnp.float32) - 0.5 * cubic)

    return body


def solution(mesh):
    return jax.shard_map(
        make_body(mesh.shape["row"], mesh.shape["col"]),
        mesh=mesh,
        in_specs=(P("row", "col"), P()),
        out_specs=P("row", "col"),
        check_vma=False,
    )
```

```python
import jax
import jax.numpy as jnp
from jax import lax
from jax.sharding import PartitionSpec as P

B = 128


def _swap(x, axis, size, d):
    return lax.ppermute(x, axis, [(i, i ^ d) for i in range(size)])


def make_body(n_row, n_col):
    n_z = n_col // 2

    def body(matrix_in, pattern):
        rows, cols = matrix_in.shape
        ratio = rows // cols
        block_rows = rows // B
        block_cols = cols // B
        row_index = lax.axis_index("row")
        col_index = lax.axis_index("col")
        local_blocks = lax.dynamic_slice(
            pattern, (row_index * block_rows, col_index * block_cols), (block_rows, block_cols)
        )
        local_mask = jnp.repeat(jnp.repeat(local_blocks, B, axis=0), B, axis=1)
        masked = matrix_in * local_mask.astype(jnp.bfloat16)

        col_pieces = [masked] + [_swap(masked, "row", n_row, j) for j in range(1, n_row)]

        col_pieces = [masked] + [_swap(masked, "row", n_row, j) for j in range(1, n_row)]

        members = jnp.arange(n_z, dtype=jnp.int32) * 2
        slots = jnp.concatenate([members, members + 1]) ^ col_index
        sub_index = ((slots // ratio) ^ row_index) * ratio + slots % ratio

        def in_slot_order(pieces):
            stacked = jnp.stack(pieces).reshape(n_row * ratio, cols, cols)
            return jnp.take(stacked, sub_index, axis=0).reshape(n_col * cols, cols)

        col_slot = None
        mask_float = local_mask.astype(jnp.float32)
        waves = 2 if rows % (2 * B) == 0 else 1
        half = rows // waves
        row_cats, f_waves = [], []
        previous = None
        for w in range(waves):
            part = masked[w * half:(w + 1) * half]
            if previous is not None:
                part, _ = lax.optimization_barrier((part, previous))
            own = jnp.concatenate(
                [part] + [_swap(part, "col", n_col, 2 * k) for k in range(1, n_z)], axis=1
            )
            row_cat = jnp.concatenate([own, _swap(own, "col", n_col, 1)], axis=1)
            row_cats.append(row_cat)
            if col_slot is None:
                col_slot = in_slot_order(col_pieces)
            square = jnp.dot(row_cat, col_slot, preferred_element_type=jnp.float32)
            filtered = (mask_float[w * half:(w + 1) * half] * square).astype(jnp.bfloat16)
            previous = filtered
            f_wave = [filtered] + [None] * (n_row - 1)
            if w + 1 < waves:
                step = 1
                while step < n_row:
                    got = _swap(jnp.stack(f_wave[:step]), "row", n_row, step)
                    for j in range(step):
                        f_wave[j ^ step] = got[j]
                    step *= 2
            else:
                for j in range(1, n_row):
                    f_wave[j] = _swap(filtered, "row", n_row, j)
            f_waves.append(f_wave)

        f_pieces = [jnp.concatenate([fw[j] for fw in f_waves], axis=0) for j in range(n_row)]
        f_slot = in_slot_order(f_pieces)
        cubic = jnp.concatenate(
            [jnp.dot(rc, f_slot, preferred_element_type=jnp.float32) for rc in row_cats], axis=0
        )
        return mask_float * (1.5 * masked.astype(jnp.float32) - 0.5 * cubic)

    return body


def solution(mesh):
    return jax.shard_map(
        make_body(mesh.shape["row"], mesh.shape["col"]),
        mesh=mesh,
        in_specs=(P("row", "col"), P()),
        out_specs=P("row", "col"),
        check_vma=False,
    )
```

```python
import jax
import jax.numpy as jnp
from jax import lax
from jax.sharding import PartitionSpec as P

B = 128


def _swap(x, axis, size, d):
    return lax.ppermute(x, axis, [(i, i ^ d) for i in range(size)])


def make_body(n_row, n_col):
    n_z = n_col // 2

    def body(matrix_in, pattern):
        rows, cols = matrix_in.shape
        ratio = rows // cols
        block_rows = rows // B
        block_cols = cols // B
        row_index = lax.axis_index("row")
        col_index = lax.axis_index("col")
        local_blocks = lax.dynamic_slice(
            pattern, (row_index * block_rows, col_index * block_cols), (block_rows, block_cols)
        )
        local_mask = jnp.repeat(jnp.repeat(local_blocks, B, axis=0), B, axis=1)
        masked = matrix_in * local_mask.astype(jnp.bfloat16)

        col_pieces = [masked] + [_swap(masked, "row", n_row, j) for j in range(1, n_row)]

        late, _ = lax.optimization_barrier((masked, col_pieces[1]))
        row_pieces = [None] * n_col
        row_pieces[0] = masked
        row_pieces[1] = _swap(late, "col", n_col, 1)
        for k in range(1, n_z):
            piece = _swap(late if k == 1 else masked, "col", n_col, 2 * k)
            row_pieces[2 * k] = piece
            row_pieces[2 * k + 1] = _swap(piece, "col", n_col, 1)

        slots = jnp.arange(n_col, dtype=jnp.int32) ^ col_index
        sub_index = ((slots // ratio) ^ row_index) * ratio + slots % ratio

        def in_slot_order(pieces):
            stacked = jnp.stack(pieces).reshape(n_row * ratio, cols, cols)
            return jnp.take(stacked, sub_index, axis=0).reshape(n_col * cols, cols)

        row_cat = jnp.concatenate(row_pieces, axis=1)
        square = jnp.dot(row_cat, in_slot_order(col_pieces), preferred_element_type=jnp.float32)
        mask_float = local_mask.astype(jnp.float32)
        filtered = (mask_float * square).astype(jnp.bfloat16)
        f_pieces = [filtered] + [_swap(filtered, "row", n_row, k) for k in range(1, n_row)]
        cubic = None
        for j, f_piece in enumerate(f_pieces):
            for h in range(ratio):
                member = (row_index ^ j) * ratio + h
                window = lax.dynamic_slice_in_dim(row_cat, (member ^ col_index) * cols, cols, 1)
                term = jnp.dot(
                    window, f_piece[h * cols:(h + 1) * cols], preferred_element_type=jnp.float32
                )
                cubic = term if cubic is None else cubic + term
        return mask_float * (1.5 * masked.astype(jnp.float32) - 0.5 * cubic)

    return body


def solution(mesh):
    return jax.shard_map(
        make_body(mesh.shape["row"], mesh.shape["col"]),
        mesh=mesh,
        in_specs=(P("row", "col"), P()),
        out_specs=P("row", "col"),
        check_vma=False,
    )
```

```python
import jax
import jax.numpy as jnp
from jax import lax
from jax.sharding import PartitionSpec as P

B = 128


def _swap(x, axis, size, d):
    return lax.ppermute(x, axis, [(i, i ^ d) for i in range(size)])


def make_body(n_row, n_col):
    n_z = n_col // 2

    def body(matrix_in, pattern):
        rows, cols = matrix_in.shape
        ratio = rows // cols
        block_rows = rows // B
        block_cols = cols // B
        row_index = lax.axis_index("row")
        col_index = lax.axis_index("col")
        local_blocks = lax.dynamic_slice(
            pattern, (row_index * block_rows, col_index * block_cols), (block_rows, block_cols)
        )
        local_mask = jnp.repeat(jnp.repeat(local_blocks, B, axis=0), B, axis=1)
        masked = matrix_in * local_mask.astype(jnp.bfloat16)
        keep = pattern.astype(jnp.bfloat16)

        def mask_from(x, row_member, col_member):
            blocks = lax.dynamic_slice(
                keep, (row_member * block_rows, col_member * block_cols), (block_rows, block_cols)
            )
            x4 = x.reshape(block_rows, B, block_cols, B)
            return (x4 * blocks[:, None, :, None]).reshape(rows, cols)


        col_raw = [None] + [_swap(matrix_in, "row", n_row, j) for j in range(1, n_row)]
        col_pieces = [masked] + [
            mask_from(col_raw[j], row_index ^ j, col_index) for j in range(1, n_row)
        ]

        late, _ = lax.optimization_barrier((matrix_in, col_raw[1]))
        raw = [None] * n_col
        raw[1] = _swap(late, "col", n_col, 1)
        for k in range(1, n_z):
            piece = _swap(late if k == 1 else matrix_in, "col", n_col, 2 * k)
            raw[2 * k] = piece
            raw[2 * k + 1] = _swap(piece, "col", n_col, 1)
        row_pieces = [masked] + [mask_from(raw[t], row_index, col_index ^ t) for t in range(1, n_col)]

        slots = jnp.arange(n_col, dtype=jnp.int32) ^ col_index
        sub_index = ((slots // ratio) ^ row_index) * ratio + slots % ratio

        def in_slot_order(pieces):
            stacked = jnp.stack(pieces).reshape(n_row * ratio, cols, cols)
            return jnp.take(stacked, sub_index, axis=0).reshape(n_col * cols, cols)

        row_cat = jnp.concatenate(row_pieces, axis=1)
        square = jnp.dot(row_cat, in_slot_order(col_pieces), preferred_element_type=jnp.float32)
        mask_float = local_mask.astype(jnp.float32)
        filtered = (mask_float * square).astype(jnp.bfloat16)
        f_pieces = [filtered] + [_swap(filtered, "row", n_row, k) for k in range(1, n_row)]
        f_slot = in_slot_order(f_pieces)
        cubic = jnp.dot(row_cat, f_slot, preferred_element_type=jnp.float32)
        return mask_float * (1.5 * masked.astype(jnp.float32) - 0.5 * cubic)

    return body


def solution(mesh):
    return jax.shard_map(
        make_body(mesh.shape["row"], mesh.shape["col"]),
        mesh=mesh,
        in_specs=(P("row", "col"), P()),
        out_specs=P("row", "col"),
        check_vma=False,
    )
```

```python
import jax
import jax.numpy as jnp
from jax import lax
from jax.sharding import PartitionSpec as P

B = 128


def _swap(x, axis, size, d):
    return lax.ppermute(x, axis, [(i, i ^ d) for i in range(size)])


def make_body(n_row, n_col):
    n_z = n_col // 2

    def body(matrix_in, pattern):
        rows, cols = matrix_in.shape
        ratio = rows // cols
        block_rows = rows // B
        block_cols = cols // B
        row_index = lax.axis_index("row")
        col_index = lax.axis_index("col")
        local_blocks = lax.dynamic_slice(
            pattern, (row_index * block_rows, col_index * block_cols), (block_rows, block_cols)
        )
        local_mask = jnp.repeat(jnp.repeat(local_blocks, B, axis=0), B, axis=1)
        masked = matrix_in * local_mask.astype(jnp.bfloat16)
        keep = pattern.astype(jnp.bfloat16)

        def mask_from(x, row_member, col_member):
            blocks = lax.dynamic_slice(
                keep, (row_member * block_rows, col_member * block_cols), (block_rows, block_cols)
            )
            x4 = x.reshape(block_rows, B, block_cols, B)
            return (x4 * blocks[:, None, :, None]).reshape(rows, cols)


        col_raw = [None] + [_swap(matrix_in, "row", n_row, j) for j in range(1, n_row)]
        col_pieces = [masked] + [
            mask_from(col_raw[j], row_index ^ j, col_index) for j in range(1, n_row)
        ]

        late, _ = lax.optimization_barrier((matrix_in, col_raw[1]))
        raw = [None] * n_col
        raw[1] = _swap(late, "col", n_col, 1)
        for k in range(1, n_z):
            piece = _swap(matrix_in, "col", n_col, 2 * k)
            raw[2 * k] = piece
            raw[2 * k + 1] = _swap(piece, "col", n_col, 1)
        row_pieces = [masked] + [mask_from(raw[t], row_index, col_index ^ t) for t in range(1, n_col)]

        slots = jnp.arange(n_col, dtype=jnp.int32) ^ col_index
        sub_index = ((slots // ratio) ^ row_index) * ratio + slots % ratio

        def in_slot_order(pieces):
            stacked = jnp.stack(pieces).reshape(n_row * ratio, cols, cols)
            return jnp.take(stacked, sub_index, axis=0).reshape(n_col * cols, cols)

        row_cat = jnp.concatenate(row_pieces, axis=1)
        square = jnp.dot(row_cat, in_slot_order(col_pieces), preferred_element_type=jnp.float32)
        mask_float = local_mask.astype(jnp.float32)
        filtered = (mask_float * square).astype(jnp.bfloat16)
        f_pieces = [filtered] + [_swap(filtered, "row", n_row, k) for k in range(1, n_row)]
        f_slot = in_slot_order(f_pieces)
        cubic = jnp.dot(row_cat, f_slot, preferred_element_type=jnp.float32)
        return mask_float * (1.5 * masked.astype(jnp.float32) - 0.5 * cubic)

    return body


def solution(mesh):
    return jax.shard_map(
        make_body(mesh.shape["row"], mesh.shape["col"]),
        mesh=mesh,
        in_specs=(P("row", "col"), P()),
        out_specs=P("row", "col"),
        check_vma=False,
    )
```

```python
import jax
import jax.numpy as jnp
from jax import lax
from jax.sharding import PartitionSpec as P

B = 128


def _swap(x, axis, size, d):
    return lax.ppermute(x, axis, [(i, i ^ d) for i in range(size)])


def make_body(n_row, n_col):
    n_z = n_col // 2

    def body(matrix_in, pattern):
        rows, cols = matrix_in.shape
        ratio = rows // cols
        block_rows = rows // B
        block_cols = cols // B
        row_index = lax.axis_index("row")
        col_index = lax.axis_index("col")
        local_blocks = lax.dynamic_slice(
            pattern, (row_index * block_rows, col_index * block_cols), (block_rows, block_cols)
        )
        local_mask = jnp.repeat(jnp.repeat(local_blocks, B, axis=0), B, axis=1)
        masked = matrix_in * local_mask.astype(jnp.bfloat16)
        keep = pattern.astype(jnp.bfloat16)

        def mask_from(x, row_member, col_member):
            blocks = lax.dynamic_slice(
                keep, (row_member * block_rows, col_member * block_cols), (block_rows, block_cols)
            )
            x4 = x.reshape(block_rows, B, block_cols, B)
            return (x4 * blocks[:, None, :, None]).reshape(rows, cols)


        raw = [None] * n_col
        for k in range(1, n_z):
            raw[2 * k] = _swap(matrix_in, "col", n_col, 2 * k)
        first_src = lax.optimization_barrier((matrix_in, raw[2]))[0] if n_z > 1 else matrix_in
        col_raw = [None] + [
            _swap(first_src if j == 1 else matrix_in, "row", n_row, j) for j in range(1, n_row)
        ]
        late = lax.optimization_barrier((matrix_in, col_raw[1]))[0] if n_row > 1 else matrix_in
        col_pieces = [masked] + [
            mask_from(col_raw[j], row_index ^ j, col_index) for j in range(1, n_row)
        ]
        raw[1] = _swap(late, "col", n_col, 1)
        for k in range(1, n_z):
            raw[2 * k + 1] = _swap(raw[2 * k], "col", n_col, 1)
        row_pieces = [masked] + [mask_from(raw[t], row_index, col_index ^ t) for t in range(1, n_col)]

        slots = jnp.arange(n_col, dtype=jnp.int32) ^ col_index
        sub_index = ((slots // ratio) ^ row_index) * ratio + slots % ratio

        def in_slot_order(pieces):
            stacked = jnp.stack(pieces).reshape(n_row * ratio, cols, cols)
            return jnp.take(stacked, sub_index, axis=0).reshape(n_col * cols, cols)

        row_cat = jnp.concatenate(row_pieces, axis=1)
        square = jnp.dot(row_cat, in_slot_order(col_pieces), preferred_element_type=jnp.float32)
        mask_float = local_mask.astype(jnp.float32)
        filtered = (mask_float * square).astype(jnp.bfloat16)
        f_pieces = [filtered] + [_swap(filtered, "row", n_row, k) for k in range(1, n_row)]
        f_slot = in_slot_order(f_pieces)
        cubic = jnp.dot(row_cat, f_slot, preferred_element_type=jnp.float32)
        return mask_float * (1.5 * masked.astype(jnp.float32) - 0.5 * cubic)

    return body


def solution(mesh):
    return jax.shard_map(
        make_body(mesh.shape["row"], mesh.shape["col"]),
        mesh=mesh,
        in_specs=(P("row", "col"), P()),
        out_specs=P("row", "col"),
        check_vma=False,
    )
```

```python
import jax
import jax.numpy as jnp
from jax import lax
from jax.sharding import PartitionSpec as P

B = 128


def _swap(x, axis, size, d):
    return lax.ppermute(x, axis, [(i, i ^ d) for i in range(size)])


def make_body(n_row, n_col):
    n_z = n_col // 2

    def body(matrix_in, pattern):
        rows, cols = matrix_in.shape
        ratio = rows // cols
        block_rows = rows // B
        block_cols = cols // B
        row_index = lax.axis_index("row")
        col_index = lax.axis_index("col")
        local_blocks = lax.dynamic_slice(
            pattern, (row_index * block_rows, col_index * block_cols), (block_rows, block_cols)
        )
        local_mask = jnp.repeat(jnp.repeat(local_blocks, B, axis=0), B, axis=1)
        masked = matrix_in * local_mask.astype(jnp.bfloat16)
        keep = pattern.astype(jnp.bfloat16)

        def mask_from(x, row_member, col_member):
            blocks = lax.dynamic_slice(
                keep, (row_member * block_rows, col_member * block_cols), (block_rows, block_cols)
            )
            x4 = x.reshape(block_rows, B, block_cols, B)
            return (x4 * blocks[:, None, :, None]).reshape(rows, cols)


        col_raw = [None] + [_swap(matrix_in, "row", n_row, j) for j in range(1, n_row)]
        col_pieces = [masked] + [
            mask_from(col_raw[j], row_index ^ j, col_index) for j in range(1, n_row)
        ]

        late, _ = lax.optimization_barrier((matrix_in, col_raw[1]))
        raw = [None] * n_col
        raw[1] = _swap(late, "col", n_col, 1)
        for k in range(1, n_z):
            piece = _swap(matrix_in, "col", n_col, 2 * k)
            raw[2 * k] = piece
            raw[2 * k + 1] = _swap(piece, "col", n_col, 1)
        row_pieces = [masked] + [mask_from(raw[t], row_index, col_index ^ t) for t in range(1, n_col)]

        slots = jnp.arange(n_col, dtype=jnp.int32) ^ col_index
        sub_index = ((slots // ratio) ^ row_index) * ratio + slots % ratio

        def in_slot_order(pieces):
            stacked = jnp.stack(pieces).reshape(n_row * ratio, cols, cols)
            return jnp.take(stacked, sub_index, axis=0).reshape(n_col * cols, cols)

        row_cat = jnp.concatenate(row_pieces, axis=1)
        square = jnp.dot(row_cat, in_slot_order(col_pieces), preferred_element_type=jnp.float32)
        mask_float = local_mask.astype(jnp.float32)
        filtered = (mask_float * square).astype(jnp.bfloat16)
        f_pieces = [filtered] + [_swap(filtered, "row", n_row, k) for k in range(1, n_row)]
        f_members = (
            (jnp.arange(n_row, dtype=jnp.int32)[:, None] ^ row_index) * ratio
            + jnp.arange(ratio, dtype=jnp.int32)[None, :]
        ).reshape(-1)
        row_f = jnp.take(row_cat.reshape(rows, n_col, cols), f_members ^ col_index, axis=1)
        row_f = row_f.reshape(rows, n_col * cols)
        f_cat = jnp.concatenate(f_pieces, axis=0)
        cubic = jnp.dot(row_f, f_cat, preferred_element_type=jnp.float32)
        return mask_float * (1.5 * masked.astype(jnp.float32) - 0.5 * cubic)

    return body


def solution(mesh):
    return jax.shard_map(
        make_body(mesh.shape["row"], mesh.shape["col"]),
        mesh=mesh,
        in_specs=(P("row", "col"), P()),
        out_specs=P("row", "col"),
        check_vma=False,
    )
```

```python
import jax
import jax.numpy as jnp
from jax import lax
from jax.sharding import PartitionSpec as P

B = 128


def _swap(x, axis, size, d):
    return lax.ppermute(x, axis, [(i, i ^ d) for i in range(size)])


def make_body(n_row, n_col):
    n_z = n_col // 2

    def body(matrix_in, pattern):
        rows, cols = matrix_in.shape
        ratio = rows // cols
        block_rows = rows // B
        block_cols = cols // B
        row_index = lax.axis_index("row")
        col_index = lax.axis_index("col")
        local_blocks = lax.dynamic_slice(
            pattern, (row_index * block_rows, col_index * block_cols), (block_rows, block_cols)
        )
        local_mask = jnp.repeat(jnp.repeat(local_blocks, B, axis=0), B, axis=1)
        masked = matrix_in * local_mask.astype(jnp.bfloat16)
        keep = pattern.astype(jnp.bfloat16)

        def mask_from(x, row_member, col_member):
            blocks = lax.dynamic_slice(
                keep, (row_member * block_rows, col_member * block_cols), (block_rows, block_cols)
            )
            x4 = x.reshape(block_rows, B, block_cols, B)
            return (x4 * blocks[:, None, :, None]).reshape(rows, cols)


        col_raw = [None] + [_swap(matrix_in, "row", n_row, j) for j in range(1, n_row)]
        col_pieces = [masked] + [
            mask_from(col_raw[j], row_index ^ j, col_index) for j in range(1, n_row)
        ]

        late, _ = lax.optimization_barrier((matrix_in, col_raw[1]))
        raw = [None] * n_col
        raw[1] = _swap(late, "col", n_col, 1)
        for k in range(1, n_z):
            piece = _swap(matrix_in, "col", n_col, 2 * k)
            raw[2 * k] = piece
            raw[2 * k + 1] = _swap(piece, "col", n_col, 1)
        row_pieces = [masked] + [mask_from(raw[t], row_index, col_index ^ t) for t in range(1, n_col)]

        slots = jnp.arange(n_col, dtype=jnp.int32) ^ col_index
        sub_index = ((slots // ratio) ^ row_index) * ratio + slots % ratio

        def in_slot_order(pieces):
            stacked = jnp.stack(pieces).reshape(n_row * ratio, cols, cols)
            picked = jnp.take(stacked, sub_index, axis=0, mode="clip")
            return picked.reshape(n_col * cols, cols)

        row_cat = jnp.concatenate(row_pieces, axis=1)
        square = jnp.dot(row_cat, in_slot_order(col_pieces), preferred_element_type=jnp.float32)
        mask_float = local_mask.astype(jnp.float32)
        filtered = (mask_float * square).astype(jnp.bfloat16)
        f_pieces = [filtered] + [_swap(filtered, "row", n_row, k) for k in range(1, n_row)]
        f_members = (
            (jnp.arange(n_row, dtype=jnp.int32)[:, None] ^ row_index) * ratio
            + jnp.arange(ratio, dtype=jnp.int32)[None, :]
        ).reshape(-1)
        row_f = jnp.take(
            row_cat.reshape(rows, n_col, cols), f_members ^ col_index, axis=1,
            mode="clip",
        )
        row_f = row_f.reshape(rows, n_col * cols)
        f_cat = jnp.concatenate(f_pieces, axis=0)
        cubic = jnp.dot(row_f, f_cat, preferred_element_type=jnp.float32)
        return mask_float * (1.5 * masked.astype(jnp.float32) - 0.5 * cubic)

    return body


def solution(mesh):
    return jax.shard_map(
        make_body(mesh.shape["row"], mesh.shape["col"]),
        mesh=mesh,
        in_specs=(P("row", "col"), P()),
        out_specs=P("row", "col"),
        check_vma=False,
    )
```

```python
import jax
import jax.numpy as jnp
from jax import lax
from jax.sharding import PartitionSpec as P

B = 128


def _swap(x, axis, size, d):
    return lax.ppermute(x, axis, [(i, i ^ d) for i in range(size)])


def make_body(n_row, n_col):
    n_z = n_col // 2

    def body(matrix_in, pattern):
        rows, cols = matrix_in.shape
        ratio = rows // cols
        block_rows = rows // B
        block_cols = cols // B
        row_index = lax.axis_index("row")
        col_index = lax.axis_index("col")
        local_blocks = lax.dynamic_slice(
            pattern, (row_index * block_rows, col_index * block_cols), (block_rows, block_cols)
        )
        local_mask = jnp.repeat(jnp.repeat(local_blocks, B, axis=0), B, axis=1)
        masked = matrix_in * local_mask.astype(jnp.bfloat16)
        keep = pattern.astype(jnp.bfloat16)

        def mask_from(x, row_member, col_member):
            blocks = lax.dynamic_slice(
                keep, (row_member * block_rows, col_member * block_cols), (block_rows, block_cols)
            )
            x4 = x.reshape(block_rows, B, block_cols, B)
            return (x4 * blocks[:, None, :, None]).reshape(rows, cols)


        col_raw = [None] + [_swap(matrix_in, "row", n_row, j) for j in range(1, n_row)]
        col_pieces = [masked] + [
            mask_from(col_raw[j], row_index ^ j, col_index) for j in range(1, n_row)
        ]

        late, _ = lax.optimization_barrier((matrix_in, col_raw[1]))
        raw = [None] * n_col
        raw[1] = _swap(late, "col", n_col, 1)
        for k in range(1, n_z):
            piece = _swap(matrix_in, "col", n_col, 2 * k)
            raw[2 * k] = piece
            raw[2 * k + 1] = _swap(piece, "col", n_col, 1)
        row_pieces = [masked] + [mask_from(raw[t], row_index, col_index ^ t) for t in range(1, n_col)]

        slots = jnp.arange(n_col, dtype=jnp.int32) ^ col_index
        sub_index = ((slots // ratio) ^ row_index) * ratio + slots % ratio

        def in_slot_order(pieces):
            stacked = jnp.stack(pieces).reshape(n_row * ratio, cols, cols)
            return jnp.take(stacked, sub_index, axis=0).reshape(n_col * cols, cols)

        row_cat = jnp.concatenate(row_pieces, axis=1)
        square = jnp.dot(row_cat, in_slot_order(col_pieces), preferred_element_type=jnp.float32)
        mask_float = local_mask.astype(jnp.float32)
        filtered = (mask_float * square).astype(jnp.bfloat16)
        f_pieces = [filtered] + [_swap(filtered, "row", n_row, k) for k in range(1, n_row)]
        f_members = (
            (jnp.arange(n_row, dtype=jnp.int32)[:, None] ^ row_index) * ratio
            + jnp.arange(ratio, dtype=jnp.int32)[None, :]
        ).reshape(-1)
        row_fs = jnp.take(jnp.stack(row_pieces), f_members ^ col_index, axis=0, mode="clip")
        f_stack = jnp.concatenate(f_pieces, axis=0).reshape(n_col, cols, cols)
        cubic = jnp.einsum("qmj,qjn->mn", row_fs, f_stack, preferred_element_type=jnp.float32)
        return mask_float * (1.5 * masked.astype(jnp.float32) - 0.5 * cubic)

    return body


def solution(mesh):
    return jax.shard_map(
        make_body(mesh.shape["row"], mesh.shape["col"]),
        mesh=mesh,
        in_specs=(P("row", "col"), P()),
        out_specs=P("row", "col"),
        check_vma=False,
    )
```

```python
import jax
import jax.numpy as jnp
from jax import lax
from jax.sharding import PartitionSpec as P

B = 128


def _swap(x, axis, size, d):
    return lax.ppermute(x, axis, [(i, i ^ d) for i in range(size)])


def make_body(n_row, n_col):
    n_z = n_col // 2

    def body(matrix_in, pattern):
        rows, cols = matrix_in.shape
        ratio = rows // cols
        block_rows = rows // B
        block_cols = cols // B
        row_index = lax.axis_index("row")
        col_index = lax.axis_index("col")
        local_blocks = lax.dynamic_slice(
            pattern, (row_index * block_rows, col_index * block_cols), (block_rows, block_cols)
        )
        local_mask = jnp.repeat(jnp.repeat(local_blocks, B, axis=0), B, axis=1)
        masked = matrix_in * local_mask.astype(jnp.bfloat16)
        keep = pattern.astype(jnp.bfloat16)

        def mask_from(x, row_member, col_member):
            blocks = lax.dynamic_slice(
                keep, (row_member * block_rows, col_member * block_cols), (block_rows, block_cols)
            )
            x4 = x.reshape(block_rows, B, block_cols, B)
            return (x4 * blocks[:, None, :, None]).reshape(rows, cols)


        col_raw = [None] + [_swap(matrix_in, "row", n_row, j) for j in range(1, n_row)]
        col_pieces = [masked] + [
            mask_from(col_raw[j], row_index ^ j, col_index) for j in range(1, n_row)
        ]

        late, _ = lax.optimization_barrier((matrix_in, col_raw[1]))
        raw = [None] * n_col
        raw[1] = _swap(late, "col", n_col, 1)
        for k in range(1, n_z):
            piece = _swap(matrix_in, "col", n_col, 2 * k)
            raw[2 * k] = piece
            raw[2 * k + 1] = _swap(piece, "col", n_col, 1)
        row_pieces = [masked] + [mask_from(raw[t], row_index, col_index ^ t) for t in range(1, n_col)]

        slots = jnp.arange(n_col, dtype=jnp.int32) ^ col_index
        sub_index = ((slots // ratio) ^ row_index) * ratio + slots % ratio

        def in_slot_order(pieces):
            stacked = jnp.stack(pieces).reshape(n_row * ratio, cols, cols)
            return jnp.take(stacked, sub_index, axis=0).reshape(n_col * cols, cols)

        row_cat = jnp.concatenate(row_pieces, axis=1)
        square = jnp.dot(row_cat, in_slot_order(col_pieces), preferred_element_type=jnp.float32)
        mask_float = local_mask.astype(jnp.float32)
        filtered = (mask_float * square).astype(jnp.bfloat16)
        f_pieces = [filtered] + [_swap(filtered, "row", n_row, k) for k in range(1, n_row)]
        f_members = (
            (jnp.arange(n_row, dtype=jnp.int32)[:, None] ^ row_index) * ratio
            + jnp.arange(ratio, dtype=jnp.int32)[None, :]
        ).reshape(-1)
        row_fs = jnp.take(jnp.stack(row_pieces), f_members ^ col_index, axis=0, mode="clip")
        cubic = None
        for j, f_piece in enumerate(f_pieces):
            term = jnp.einsum(
                "qmj,qjn->mn", row_fs[j * ratio:(j + 1) * ratio],
                f_piece.reshape(ratio, cols, cols), preferred_element_type=jnp.float32,
            )
            cubic = term if cubic is None else cubic + term
        return mask_float * (1.5 * masked.astype(jnp.float32) - 0.5 * cubic)

    return body


def solution(mesh):
    return jax.shard_map(
        make_body(mesh.shape["row"], mesh.shape["col"]),
        mesh=mesh,
        in_specs=(P("row", "col"), P()),
        out_specs=P("row", "col"),
        check_vma=False,
    )
```

```python
import jax
import jax.numpy as jnp
from jax import lax
from jax.sharding import PartitionSpec as P

B = 128


def _swap(x, axis, size, d):
    return lax.ppermute(x, axis, [(i, i ^ d) for i in range(size)])


def make_body(n_row, n_col):
    n_z = n_col // 2

    def body(matrix_in, pattern):
        rows, cols = matrix_in.shape
        ratio = rows // cols
        block_rows = rows // B
        block_cols = cols // B
        row_index = lax.axis_index("row")
        col_index = lax.axis_index("col")
        local_blocks = lax.dynamic_slice(
            pattern, (row_index * block_rows, col_index * block_cols), (block_rows, block_cols)
        )
        local_mask = jnp.repeat(jnp.repeat(local_blocks, B, axis=0), B, axis=1)
        masked = matrix_in * local_mask.astype(jnp.bfloat16)
        keep = pattern.astype(jnp.bfloat16)

        def mask_from(x, row_member, col_member):
            blocks = lax.dynamic_slice(
                keep, (row_member * block_rows, col_member * block_cols), (block_rows, block_cols)
            )
            x4 = x.reshape(block_rows, B, block_cols, B)
            return (x4 * blocks[:, None, :, None]).reshape(rows, cols)


        col_raw = [None] + [_swap(matrix_in, "row", n_row, j) for j in range(1, n_row)]
        col_pieces = [masked] + [
            mask_from(col_raw[j], row_index ^ j, col_index) for j in range(1, n_row)
        ]

        late, _ = lax.optimization_barrier((matrix_in, col_raw[1]))
        raw = [None] * n_col
        raw[1] = _swap(late, "col", n_col, 1)
        for k in range(1, n_z):
            piece = _swap(matrix_in, "col", n_col, 2 * k)
            raw[2 * k] = piece
            raw[2 * k + 1] = _swap(piece, "col", n_col, 1)
        row_pieces = [masked] + [mask_from(raw[t], row_index, col_index ^ t) for t in range(1, n_col)]

        slots = jnp.arange(n_col, dtype=jnp.int32) ^ col_index
        sub_index = ((slots // ratio) ^ row_index) * ratio + slots % ratio

        def in_slot_order(pieces):
            stacked = jnp.stack(pieces).reshape(n_row * ratio, cols, cols)
            return jnp.take(stacked, sub_index, axis=0).reshape(n_col * cols, cols)

        row_cat = jnp.concatenate(row_pieces, axis=1)
        square = jnp.dot(row_cat, in_slot_order(col_pieces), preferred_element_type=jnp.float32)
        mask_float = local_mask.astype(jnp.float32)
        filtered = (mask_float * square).astype(jnp.bfloat16)
        f_pieces = [filtered] + [_swap(filtered, "row", n_row, k) for k in range(1, n_row)]
        f_members = (
            (jnp.arange(n_row, dtype=jnp.int32)[:, None] ^ row_index) * ratio
            + jnp.arange(ratio, dtype=jnp.int32)[None, :]
        ).reshape(-1)
        row_fs = jnp.take(jnp.stack(row_pieces), f_members ^ col_index, axis=0, mode="clip")
        row_f = jnp.transpose(row_fs, (1, 0, 2)).reshape(rows, n_col * cols)
        f_cat = jnp.concatenate(f_pieces, axis=0)
        cubic = jnp.dot(row_f, f_cat, preferred_element_type=jnp.float32)
        return mask_float * (1.5 * masked.astype(jnp.float32) - 0.5 * cubic)

    return body


def solution(mesh):
    return jax.shard_map(
        make_body(mesh.shape["row"], mesh.shape["col"]),
        mesh=mesh,
        in_specs=(P("row", "col"), P()),
        out_specs=P("row", "col"),
        check_vma=False,
    )
```

```python
import jax
import jax.numpy as jnp
from jax import lax
from jax.sharding import PartitionSpec as P

B = 128


def _swap(x, axis, size, d):
    return lax.ppermute(x, axis, [(i, i ^ d) for i in range(size)])


def make_body(n_row, n_col):
    n_z = n_col // 2

    def body(matrix_in, pattern):
        rows, cols = matrix_in.shape
        ratio = rows // cols
        block_rows = rows // B
        block_cols = cols // B
        row_index = lax.axis_index("row")
        col_index = lax.axis_index("col")
        local_blocks = lax.dynamic_slice(
            pattern, (row_index * block_rows, col_index * block_cols), (block_rows, block_cols)
        )
        local_mask = jnp.repeat(jnp.repeat(local_blocks, B, axis=0), B, axis=1)
        masked = matrix_in * local_mask.astype(jnp.bfloat16)
        keep = pattern.astype(jnp.bfloat16)

        def mask_from(x, row_member, col_member):
            blocks = lax.dynamic_slice(
                keep, (row_member * block_rows, col_member * block_cols), (block_rows, block_cols)
            )
            x4 = x.reshape(block_rows, B, block_cols, B)
            return (x4 * blocks[:, None, :, None]).reshape(rows, cols)


        col_raw = [None] + [_swap(matrix_in, "row", n_row, j) for j in range(1, n_row)]
        col_pieces = [masked] + [
            mask_from(col_raw[j], row_index ^ j, col_index) for j in range(1, n_row)
        ]

        late, _ = lax.optimization_barrier((matrix_in, col_raw[1]))
        raw = [None] * n_col
        raw[1] = _swap(late, "col", n_col, 1)
        for k in range(1, n_z):
            piece = _swap(matrix_in, "col", n_col, 2 * k)
            raw[2 * k] = piece
            raw[2 * k + 1] = _swap(piece, "col", n_col, 1)
        row_pieces = [masked] + [mask_from(raw[t], row_index, col_index ^ t) for t in range(1, n_col)]

        shift = col_index ^ (row_index * ratio)
        row_f = jnp.zeros((rows, n_col * cols), matrix_in.dtype)
        for t, piece in enumerate(row_pieces):
            row_f = lax.dynamic_update_slice_in_dim(row_f, piece, (t ^ shift) * cols, 1)
        square = jnp.dot(
            row_f, jnp.concatenate(col_pieces, axis=0), preferred_element_type=jnp.float32
        )
        mask_float = local_mask.astype(jnp.float32)
        filtered = (mask_float * square).astype(jnp.bfloat16)
        f_pieces = [filtered] + [_swap(filtered, "row", n_row, k) for k in range(1, n_row)]
        cubic = jnp.dot(row_f, jnp.concatenate(f_pieces, axis=0), preferred_element_type=jnp.float32)
        return mask_float * (1.5 * masked.astype(jnp.float32) - 0.5 * cubic)

    return body


def solution(mesh):
    return jax.shard_map(
        make_body(mesh.shape["row"], mesh.shape["col"]),
        mesh=mesh,
        in_specs=(P("row", "col"), P()),
        out_specs=P("row", "col"),
        check_vma=False,
    )
```

```python
import jax
import jax.numpy as jnp
from jax import lax
from jax.sharding import PartitionSpec as P

B = 128


def _swap(x, axis, size, d):
    return lax.ppermute(x, axis, [(i, i ^ d) for i in range(size)])


def make_body(n_row, n_col):
    n_z = n_col // 2

    def body(matrix_in, pattern):
        rows, cols = matrix_in.shape
        ratio = rows // cols
        block_rows = rows // B
        block_cols = cols // B
        row_index = lax.axis_index("row")
        col_index = lax.axis_index("col")
        local_blocks = lax.dynamic_slice(
            pattern, (row_index * block_rows, col_index * block_cols), (block_rows, block_cols)
        )
        local_mask = jnp.repeat(jnp.repeat(local_blocks, B, axis=0), B, axis=1)
        masked = matrix_in * local_mask.astype(jnp.bfloat16)
        keep = pattern.astype(jnp.bfloat16)

        def mask_from(x, row_member, col_member):
            blocks = lax.dynamic_slice(
                keep, (row_member * block_rows, col_member * block_cols), (block_rows, block_cols)
            )
            x4 = x.reshape(block_rows, B, block_cols, B)
            return (x4 * blocks[:, None, :, None]).reshape(rows, cols)


        col_raw = [None] + [_swap(matrix_in, "row", n_row, j) for j in range(1, n_row)]
        col_pieces = [masked] + [
            mask_from(col_raw[j], row_index ^ j, col_index) for j in range(1, n_row)
        ]

        late, _ = lax.optimization_barrier((matrix_in, col_raw[1]))
        raw = [None] * n_col
        raw[1] = _swap(late, "col", n_col, 1)
        for k in range(1, n_z):
            piece = _swap(matrix_in, "col", n_col, 2 * k)
            raw[2 * k] = piece
            raw[2 * k + 1] = _swap(piece, "col", n_col, 1)
        row_pieces = [masked] + [mask_from(raw[t], row_index, col_index ^ t) for t in range(1, n_col)]

        shift = col_index ^ (row_index * ratio)
        row_f = jnp.zeros((rows, n_col * cols), matrix_in.dtype)
        for t, piece in enumerate(row_pieces):
            row_f = lax.dynamic_update_slice_in_dim(row_f, piece, (t ^ shift) * cols, 1)
        square = jnp.dot(
            row_f, jnp.concatenate(col_pieces, axis=0), preferred_element_type=jnp.float32
        )
        blocks_float = local_blocks.astype(jnp.float32)[:, None, :, None]

        def mask_local(x):
            return (x.reshape(block_rows, B, block_cols, B) * blocks_float).reshape(rows, cols)

        filtered = mask_local(square).astype(jnp.bfloat16)
        f_pieces = [filtered] + [_swap(filtered, "row", n_row, k) for k in range(1, n_row)]
        cubic = jnp.dot(row_f, jnp.concatenate(f_pieces, axis=0), preferred_element_type=jnp.float32)
        return mask_local(1.5 * masked.astype(jnp.float32) - 0.5 * cubic)

    return body


def solution(mesh):
    return jax.shard_map(
        make_body(mesh.shape["row"], mesh.shape["col"]),
        mesh=mesh,
        in_specs=(P("row", "col"), P()),
        out_specs=P("row", "col"),
        check_vma=False,
    )
```

```python
import jax
import jax.numpy as jnp
from jax import lax
from jax.sharding import PartitionSpec as P

B = 128


def _swap(x, axis, size, d):
    return lax.ppermute(x, axis, [(i, i ^ d) for i in range(size)])


def make_body(n_row, n_col):
    n_z = n_col // 2

    def body(matrix_in, pattern):
        rows, cols = matrix_in.shape
        ratio = rows // cols
        block_rows = rows // B
        block_cols = cols // B
        row_index = lax.axis_index("row")
        col_index = lax.axis_index("col")
        local_blocks = lax.dynamic_slice(
            pattern, (row_index * block_rows, col_index * block_cols), (block_rows, block_cols)
        )
        local_mask = jnp.repeat(jnp.repeat(local_blocks, B, axis=0), B, axis=1)
        masked = matrix_in * local_mask.astype(jnp.bfloat16)
        keep = pattern.astype(jnp.bfloat16)

        def mask_from(x, row_member, col_member):
            blocks = lax.dynamic_slice(
                keep, (row_member * block_rows, col_member * block_cols), (block_rows, block_cols)
            )
            x4 = x.reshape(block_rows, B, block_cols, B)
            return (x4 * blocks[:, None, :, None]).reshape(rows, cols)


        col_raw = [None] + [_swap(matrix_in, "row", n_row, j) for j in range(1, n_row)]
        col_pieces = [masked] + [
            mask_from(col_raw[j], row_index ^ j, col_index) for j in range(1, n_row)
        ]

        late, _ = lax.optimization_barrier((matrix_in, col_raw[1]))
        raw = [None] * n_col
        raw[1] = _swap(late, "col", n_col, 1)
        for k in range(1, n_z):
            piece = _swap(matrix_in, "col", n_col, 2 * k)
            raw[2 * k] = piece
            raw[2 * k + 1] = _swap(piece, "col", n_col, 1)
        row_pieces = [masked] + [mask_from(raw[t], row_index, col_index ^ t) for t in range(1, n_col)]

        shift = col_index ^ (row_index * ratio)
        row_f = jnp.zeros((rows, n_col * cols), matrix_in.dtype)
        order = [t for t in range(n_col) if t not in (4, 5)] + [t for t in (4, 5) if t < n_col]
        for t in order:
            row_f = lax.dynamic_update_slice_in_dim(row_f, row_pieces[t], (t ^ shift) * cols, 1)
        square = jnp.dot(
            row_f, jnp.concatenate(col_pieces, axis=0), preferred_element_type=jnp.float32
        )
        blocks_float = local_blocks.astype(jnp.float32)[:, None, :, None]

        def mask_local(x):
            return (x.reshape(block_rows, B, block_cols, B) * blocks_float).reshape(rows, cols)

        filtered = mask_local(square).astype(jnp.bfloat16)
        f_pieces = [filtered] + [_swap(filtered, "row", n_row, k) for k in range(1, n_row)]
        cubic = jnp.dot(row_f, jnp.concatenate(f_pieces, axis=0), preferred_element_type=jnp.float32)
        return mask_local(1.5 * masked.astype(jnp.float32) - 0.5 * cubic)

    return body


def solution(mesh):
    return jax.shard_map(
        make_body(mesh.shape["row"], mesh.shape["col"]),
        mesh=mesh,
        in_specs=(P("row", "col"), P()),
        out_specs=P("row", "col"),
        check_vma=False,
    )
```

```python
import jax
import jax.numpy as jnp
from jax import lax
from jax.sharding import PartitionSpec as P

B = 128


def _swap(x, axis, size, d):
    return lax.ppermute(x, axis, [(i, i ^ d) for i in range(size)])


def make_body(n_row, n_col):
    n_z = n_col // 2

    def body(matrix_in, pattern):
        rows, cols = matrix_in.shape
        ratio = rows // cols
        block_rows = rows // B
        block_cols = cols // B
        row_index = lax.axis_index("row")
        col_index = lax.axis_index("col")
        local_blocks = lax.dynamic_slice(
            pattern, (row_index * block_rows, col_index * block_cols), (block_rows, block_cols)
        )
        local_mask = jnp.repeat(jnp.repeat(local_blocks, B, axis=0), B, axis=1)
        masked = matrix_in * local_mask.astype(jnp.bfloat16)
        keep = pattern.astype(jnp.bfloat16)

        def mask_from(x, row_member, col_member):
            blocks = lax.dynamic_slice(
                keep, (row_member * block_rows, col_member * block_cols), (block_rows, block_cols)
            )
            x4 = x.reshape(block_rows, B, block_cols, B)
            return (x4 * blocks[:, None, :, None]).reshape(rows, cols)


        col_raw = [None] + [_swap(matrix_in, "row", n_row, j) for j in range(1, n_row)]
        col_pieces = [masked] + [
            mask_from(col_raw[j], row_index ^ j, col_index) for j in range(1, n_row)
        ]

        raw = [None] * n_col
        for k in range(1, n_z):
            piece = _swap(matrix_in, "col", n_col, 2 * k)
            raw[2 * k] = piece
            raw[2 * k + 1] = _swap(piece, "col", n_col, 1)
        late = matrix_in
        if n_z > 1:
            late, _ = lax.optimization_barrier((matrix_in, raw[2 * (n_z - 1)]))
        raw[1] = _swap(late, "col", n_col, 1)
        row_pieces = [masked] + [mask_from(raw[t], row_index, col_index ^ t) for t in range(1, n_col)]

        shift = col_index ^ (row_index * ratio)
        row_f = jnp.zeros((rows, n_col * cols), matrix_in.dtype)
        for t, piece in enumerate(row_pieces):
            row_f = lax.dynamic_update_slice_in_dim(row_f, piece, (t ^ shift) * cols, 1)
        square = jnp.dot(
            row_f, jnp.concatenate(col_pieces, axis=0), preferred_element_type=jnp.float32
        )
        blocks_float = local_blocks.astype(jnp.float32)[:, None, :, None]

        def mask_local(x):
            return (x.reshape(block_rows, B, block_cols, B) * blocks_float).reshape(rows, cols)

        filtered = mask_local(square).astype(jnp.bfloat16)
        f_pieces = [filtered] + [_swap(filtered, "row", n_row, k) for k in range(1, n_row)]
        cubic = jnp.dot(row_f, jnp.concatenate(f_pieces, axis=0), preferred_element_type=jnp.float32)
        return mask_local(1.5 * masked.astype(jnp.float32) - 0.5 * cubic)

    return body


def solution(mesh):
    return jax.shard_map(
        make_body(mesh.shape["row"], mesh.shape["col"]),
        mesh=mesh,
        in_specs=(P("row", "col"), P()),
        out_specs=P("row", "col"),
        check_vma=False,
    )
```

```python
import jax
import jax.numpy as jnp
from jax import lax
from jax.sharding import PartitionSpec as P

B = 128


def _swap(x, axis, size, d):
    return lax.ppermute(x, axis, [(i, i ^ d) for i in range(size)])


def make_body(n_row, n_col):
    n_z = n_col // 2

    def body(matrix_in, pattern):
        rows, cols = matrix_in.shape
        ratio = rows // cols
        block_rows = rows // B
        block_cols = cols // B
        row_index = lax.axis_index("row")
        col_index = lax.axis_index("col")
        local_blocks = lax.dynamic_slice(
            pattern, (row_index * block_rows, col_index * block_cols), (block_rows, block_cols)
        )
        local_mask = jnp.repeat(jnp.repeat(local_blocks, B, axis=0), B, axis=1)
        masked = matrix_in * local_mask.astype(jnp.bfloat16)
        keep = pattern.astype(jnp.bfloat16)

        def mask_from(x, row_member, col_member):
            blocks = lax.dynamic_slice(
                keep, (row_member * block_rows, col_member * block_cols), (block_rows, block_cols)
            )
            x4 = x.reshape(block_rows, B, block_cols, B)
            return (x4 * blocks[:, None, :, None]).reshape(rows, cols)


        col_raw = [None] + [_swap(matrix_in, "row", n_row, j) for j in range(1, n_row)]
        col_pieces = [masked] + [
            mask_from(col_raw[j], row_index ^ j, col_index) for j in range(1, n_row)
        ]

        late, _ = lax.optimization_barrier((matrix_in, col_raw[1]))
        raw = [None] * n_col
        raw[1] = _swap(late, "col", n_col, 1)
        for k in range(1, n_z):
            piece = _swap(matrix_in, "col", n_col, 2 * k)
            raw[2 * k] = piece
            raw[2 * k + 1] = _swap(piece, "col", n_col, 1)
        row_pieces = [masked] + [mask_from(raw[t], row_index, col_index ^ t) for t in range(1, n_col)]
        if n_col > 5:
            early = [t for t in range(1, n_col) if t not in (4, 5)]
            tied = lax.optimization_barrier(
                (row_pieces[4], row_pieces[5], [row_pieces[t] for t in early], col_pieces)
            )
            row_pieces[4], row_pieces[5] = tied[0], tied[1]
            for t, piece in zip(early, tied[2]):
                row_pieces[t] = piece
            col_pieces = list(tied[3])

        shift = col_index ^ (row_index * ratio)
        row_f = jnp.zeros((rows, n_col * cols), matrix_in.dtype)
        for t, piece in enumerate(row_pieces):
            row_f = lax.dynamic_update_slice_in_dim(row_f, piece, (t ^ shift) * cols, 1)
        square = jnp.dot(
            row_f, jnp.concatenate(col_pieces, axis=0), preferred_element_type=jnp.float32
        )
        blocks_float = local_blocks.astype(jnp.float32)[:, None, :, None]

        def mask_local(x):
            return (x.reshape(block_rows, B, block_cols, B) * blocks_float).reshape(rows, cols)

        filtered = mask_local(square).astype(jnp.bfloat16)
        f_pieces = [filtered] + [_swap(filtered, "row", n_row, k) for k in range(1, n_row)]
        cubic = jnp.dot(row_f, jnp.concatenate(f_pieces, axis=0), preferred_element_type=jnp.float32)
        return mask_local(1.5 * masked.astype(jnp.float32) - 0.5 * cubic)

    return body


def solution(mesh):
    return jax.shard_map(
        make_body(mesh.shape["row"], mesh.shape["col"]),
        mesh=mesh,
        in_specs=(P("row", "col"), P()),
        out_specs=P("row", "col"),
        check_vma=False,
    )
```

```python
import jax
import jax.numpy as jnp
from jax import lax
from jax.sharding import PartitionSpec as P

B = 128


def _swap(x, axis, size, d):
    return lax.ppermute(x, axis, [(i, i ^ d) for i in range(size)])


def make_body(n_row, n_col):
    n_z = n_col // 2

    def body(matrix_in, pattern):
        rows, cols = matrix_in.shape
        ratio = rows // cols
        block_rows = rows // B
        block_cols = cols // B
        row_index = lax.axis_index("row")
        col_index = lax.axis_index("col")
        local_blocks = lax.dynamic_slice(
            pattern, (row_index * block_rows, col_index * block_cols), (block_rows, block_cols)
        )
        local_mask = jnp.repeat(jnp.repeat(local_blocks, B, axis=0), B, axis=1)
        masked = matrix_in * local_mask.astype(jnp.bfloat16)
        keep = pattern.astype(jnp.bfloat16)

        def mask_from(x, row_member, col_member):
            blocks = lax.dynamic_slice(
                keep, (row_member * block_rows, col_member * block_cols), (block_rows, block_cols)
            )
            x4 = x.reshape(block_rows, B, block_cols, B)
            return (x4 * blocks[:, None, :, None]).reshape(rows, cols)


        col_raw = [None] + [_swap(matrix_in, "row", n_row, j) for j in range(1, n_row)]
        col_pieces = [masked] + [
            mask_from(col_raw[j], row_index ^ j, col_index) for j in range(1, n_row)
        ]

        late, _ = lax.optimization_barrier((matrix_in, col_raw[1]))
        raw = [None] * n_col
        raw[1] = _swap(late, "col", n_col, 1)
        for k in range(1, n_z):
            piece = _swap(matrix_in, "col", n_col, 2 * k)
            raw[2 * k] = piece
            raw[2 * k + 1] = _swap(piece, "col", n_col, 1)
        row_pieces = [masked] + [mask_from(raw[t], row_index, col_index ^ t) for t in range(1, n_col)]
        shift = col_index ^ (row_index * ratio)
        col_cat = jnp.concatenate(col_pieces, axis=0)
        row_f = jnp.zeros((rows, n_col * cols), matrix_in.dtype)
        last = [t for t in (4, 5) if n_col > 5]
        for t in range(n_col):
            if t not in last:
                row_f = lax.dynamic_update_slice_in_dim(row_f, row_pieces[t], (t ^ shift) * cols, 1)
        square = jnp.dot(row_f, col_cat, preferred_element_type=jnp.float32)
        if last:
            tied = lax.optimization_barrier(([row_pieces[t] for t in last], row_f, square))
            row_f, square = tied[1], tied[2]
            for t, piece in zip(last, tied[0]):
                rows_t = lax.dynamic_slice_in_dim(col_cat, (t ^ shift) * cols, cols, 0)
                square = square + jnp.dot(piece, rows_t, preferred_element_type=jnp.float32)
                row_f = lax.dynamic_update_slice_in_dim(row_f, piece, (t ^ shift) * cols, 1)
        blocks_float = local_blocks.astype(jnp.float32)[:, None, :, None]

        def mask_local(x):
            return (x.reshape(block_rows, B, block_cols, B) * blocks_float).reshape(rows, cols)

        filtered = mask_local(square).astype(jnp.bfloat16)
        f_pieces = [filtered] + [_swap(filtered, "row", n_row, k) for k in range(1, n_row)]
        cubic = jnp.dot(row_f, jnp.concatenate(f_pieces, axis=0), preferred_element_type=jnp.float32)
        return mask_local(1.5 * masked.astype(jnp.float32) - 0.5 * cubic)

    return body


def solution(mesh):
    return jax.shard_map(
        make_body(mesh.shape["row"], mesh.shape["col"]),
        mesh=mesh,
        in_specs=(P("row", "col"), P()),
        out_specs=P("row", "col"),
        check_vma=False,
    )
```

```python
import jax
import jax.numpy as jnp
from jax import lax
from jax.sharding import PartitionSpec as P

B = 128


def _swap(x, axis, size, d):
    return lax.ppermute(x, axis, [(i, i ^ d) for i in range(size)])


def make_body(n_row, n_col):
    n_z = n_col // 2

    def body(matrix_in, pattern):
        rows, cols = matrix_in.shape
        ratio = rows // cols
        block_rows = rows // B
        block_cols = cols // B
        row_index = lax.axis_index("row")
        col_index = lax.axis_index("col")
        local_blocks = lax.dynamic_slice(
            pattern, (row_index * block_rows, col_index * block_cols), (block_rows, block_cols)
        )
        local_mask = jnp.repeat(jnp.repeat(local_blocks, B, axis=0), B, axis=1)
        masked = matrix_in * local_mask.astype(jnp.bfloat16)
        keep = pattern.astype(jnp.bfloat16)

        def mask_from(x, row_member, col_member):
            blocks = lax.dynamic_slice(
                keep, (row_member * block_rows, col_member * block_cols), (block_rows, block_cols)
            )
            x4 = x.reshape(block_rows, B, block_cols, B)
            return (x4 * blocks[:, None, :, None]).reshape(rows, cols)


        col_raw = [None] + [_swap(matrix_in, "row", n_row, j) for j in range(1, n_row)]
        col_pieces = [masked] + [
            mask_from(col_raw[j], row_index ^ j, col_index) for j in range(1, n_row)
        ]

        late, _ = lax.optimization_barrier((matrix_in, col_raw[1]))
        raw = [None] * n_col
        raw[1] = _swap(late, "col", n_col, 1)
        for k in range(1, n_z):
            piece = _swap(matrix_in, "col", n_col, 2 * k)
            raw[2 * k] = piece
            raw[2 * k + 1] = _swap(piece, "col", n_col, 1)
        row_pieces = [masked] + [mask_from(raw[t], row_index, col_index ^ t) for t in range(1, n_col)]
        mask_float = jnp.broadcast_to(
            local_blocks.astype(jnp.float32)[:, None, :, None], (block_rows, B, block_cols, B)
        )
        if n_col > 5:
            early = [t for t in range(1, n_col) if t not in (4, 5)]
            tied = lax.optimization_barrier(
                (row_pieces[4], row_pieces[5], [row_pieces[t] for t in early], col_pieces,
                 mask_float)
            )
            row_pieces[4], row_pieces[5] = tied[0], tied[1]
            for t, piece in zip(early, tied[2]):
                row_pieces[t] = piece
            col_pieces = list(tied[3])
            mask_float = tied[4]

        shift = col_index ^ (row_index * ratio)
        row_f = jnp.zeros((rows, n_col * cols), matrix_in.dtype)
        for t, piece in enumerate(row_pieces):
            row_f = lax.dynamic_update_slice_in_dim(row_f, piece, (t ^ shift) * cols, 1)
        square = jnp.dot(
            row_f, jnp.concatenate(col_pieces, axis=0), preferred_element_type=jnp.float32
        )
        def mask_local(x):
            return (x.reshape(block_rows, B, block_cols, B) * mask_float).reshape(rows, cols)

        filtered = mask_local(square).astype(jnp.bfloat16)
        f_pieces = [filtered] + [_swap(filtered, "row", n_row, k) for k in range(1, n_row)]
        cubic = jnp.dot(row_f, jnp.concatenate(f_pieces, axis=0), preferred_element_type=jnp.float32)
        return mask_local(1.5 * masked.astype(jnp.float32) - 0.5 * cubic)

    return body


def solution(mesh):
    return jax.shard_map(
        make_body(mesh.shape["row"], mesh.shape["col"]),
        mesh=mesh,
        in_specs=(P("row", "col"), P()),
        out_specs=P("row", "col"),
        check_vma=False,
    )
```
